256 devices in a mesh: dp: 64 (over z, y, core), mp: 4 (over x).
Axes of the slice: x: 4, y: 4, z: 8, core: 2. Of those that a mesh axis runs over, the one named last changes fastest.
Arguments:
- acts: bfloat16 [114688, 768], P('dp'), may hold values from -250 to 250
- proj_cotangent: bfloat16 [114688, 3352], P('dp', 'mp'), may hold values from -6 to 6
- inner_acts: bfloat16 [114688, 1536], P('dp', 'mp'), may hold values from -6 to 6
- out_cotangent: bfloat16 [114688, 768], P('dp'), may hold values from -6 to 6
- in_master: float32 [768, 3352], P('dp', 'mp'), may hold values from -0.21875 to 0.21875
- in_first: float32 [768, 3352], P('dp', 'mp'), may hold values from -0.0029296875 to 0.0029296875
- in_second: float32 [768, 3352], P('dp', 'mp'), may hold values from 1e-08 to 1e-06
- out_master: float32 [1536, 768], P('mp', 'dp'), may hold values from -0.15625 to 0.15625
- out_first: float32 [1536, 768], P('mp', 'dp'), may hold values from -0.0029296875 to 0.0029296875
- out_second: float32 [1536, 768], P('mp', 'dp'), may hold values from 1e-08 to 1e-06
- conv_grads: float32 [64, 2, 5, 1792], P('dp', None, None, 'mp'), may hold values from -1800 to 1800
- conv_master: float32 [5, 1792], P(None, 'mp'), may hold values from -3 to 3
- conv_first: float32 [5, 1792], P(None, 'mp'), may hold values from -0.0029296875 to 0.0029296875
- conv_second: float32 [5, 1792], P(None, 'mp'), may hold values from 1e-06 to 0.01
- head_grads: float32 [64, 2, 24, 67], P('dp', None, 'mp'), may hold values from -1800 to 1800
- head_master: float32 [24, 67], P('mp'), may hold values from 0.5 to 2
- head_first: float32 [24, 67], P('mp'), may hold values from -0.0029296875 to 0.0029296875
- head_second: float32 [24, 67], P('mp'), may hold values from 1e-06 to 0.01
- gain_grads: float32 [64, 2, 4, 768], P('dp', None, 'mp'), may hold values from -1800 to 1800
- gain_master: float32 [768], replicated, may hold values from 0.5 to 1.5
- gain_first: float32 [768], replicated, may hold values from -0.0029296875 to 0.0029296875
- gain_second: float32 [768], replicated, may hold values from 1e-06 to 0.01
Outputs:
- in_master_new: float32 [768, 3352], P('dp', 'mp')
- in_first_new: float32 [768, 3352], P('dp', 'mp')
- in_second_new: float32 [768, 3352], P('dp', 'mp')
- in_weights: bfloat16 [768, 3352], P(None, 'mp')
- out_master_new: float32 [1536, 768], P('mp', 'dp')
- out_first_new: float32 [1536, 768], P('mp', 'dp')
- out_second_new: float32 [1536, 768], P('mp', 'dp')
- out_weights: bfloat16 [1536, 768], P('mp')
- conv_master_new: float32 [5, 1792], P(None, 'mp')
- conv_first_new: float32 [5, 1792], P(None, 'mp')
- conv_second_new: float32 [5, 1792], P(None, 'mp')
- head_master_new: float32 [24, 67], P('mp')
- head_first_new: float32 [24, 67], P('mp')
- head_second_new: float32 [24, 67], P('mp')
- gain_master_new: float32 [768], replicated
- gain_first_new: float32 [768], replicated
- gain_second_new: float32 [768], replicated
The draws below stay inside these ranges and needn't reach their ends.
All inputs are finite; a program needn't handle non-finite values.
Results may differ from the reference program's by a relative error of at most 0.0004.
Values may be sent and summed in bfloat16 or wider, within the bound.
No kernel may reach another device: no remote copies, remote signals or barrier semaphores. Data moves between devices by JAX's collectives and lax.ppermute only.
A program may use at most 64 MiB of HBM per device.

```python
import math
import jax
import jax.numpy as jnp
from jax import lax

D = 768
INNER = 1536
HEADS = 24
KCONV = 4
MICRO = 2
PROJ = 3352
CONV = 1792
HEADDIM = 64
TOKENS = 114688
N_DP = 64
N_MP = 4


def draw_acts(key, part):
    key_base, key_jitter = jax.random.split(key, 2)
    ramp = 10.0 ** (jnp.arange(D, dtype=jnp.float32) / (D - 1))
    jitter = jnp.exp(jax.random.uniform(key_jitter, (D,), jnp.float32, -0.7, 0.7))
    base = jax.random.normal(key_base, (TOKENS, D), jnp.float32)
    return (base * ramp * jitter).astype(jnp.bfloat16)


def shared_partials(base_key, whole_shape, mean_shape):
    key_noise, key_mean = jax.random.split(base_key)
    noise_part = 300.0 * jax.random.normal(key_noise, whole_shape, jnp.float32)
    spread = 120.0
    mean_part = spread * jax.random.normal(key_mean, mean_shape, jnp.float32)
    return jnp.clip(noise_part + mean_part, -1800.0, 1800.0)


def draw_conv_grads(key, part):
    base_key = jax.random.fold_in(key, 11)
    return shared_partials(base_key, (N_DP, MICRO, KCONV + 1, CONV), (1, 1, KCONV + 1, CONV))


def draw_head_grads(key, part):
    base_key = jax.random.fold_in(key, 12)
    return shared_partials(base_key, (N_DP, MICRO, HEADS, HEADDIM + 3), (1, 1, HEADS, HEADDIM + 3))


def draw_gain_grads(key, part):
    base_key = jax.random.fold_in(key, 13)
    return shared_partials(base_key, (N_DP, MICRO, N_MP, D), (1, 1, 1, D))


def steps_of(key, shape, pieces, least, top_value):
    level = 1.0
    for position, shards_of in pieces:
        draws = jax.random.uniform(jax.random.fold_in(jax.random.fold_in(key, 6), position), (shards_of,), jnp.float32, least / len(pieces), top_value / len(pieces))
        level = level * jnp.repeat(jnp.exp(draws), shape[position] // shards_of).reshape((-1,) + (1,) * (len(shape) - 1 - position))
    return level


def scatter_about(own_key, extent, deviation, bound, cuts=(), held_as=jnp.bfloat16):
    array = jax.random.normal(own_key, extent, jnp.float32) * deviation
    if len(cuts) > 0:
        array = steps_of(own_key, extent, cuts, -0.22, 0.18) * array
    return jnp.clip(array, min=-bound, max=bound).astype(held_as)


def setup_inputs(seed: int = 0) -> dict:
    splits = jax.random.split(jax.random.key(seed), 23)
    acts = draw_acts(jax.random.fold_in(splits[22], 71), 0)
    proj_cotangent = scatter_about(splits[1], (TOKENS, PROJ), 1.0, 6.0, ((0, 64), (1, 4)))
    inner_acts = scatter_about(splits[2], (TOKENS, INNER), 1.0, 6.0, ((0, 64), (1, 4)))
    out_cotangent = scatter_about(splits[3], (TOKENS, D), 1.0, 6.0, ((0, 64),))
    in_master = scatter_about(splits[4], (D, PROJ), D ** -0.5, 0.21875, ((0, 64), (1, 4)), jnp.float32)
    in_first = scatter_about(splits[5], (D, PROJ), 0.0005, 0.0029296875, ((0, 64), (1, 4)), jnp.float32)
    in_second = jnp.clip(jnp.exp(math.log(9.999999974752427e-07) - 4.6051702 * jax.random.uniform(splits[6], (D, PROJ), jnp.float32) ** steps_of(splits[6], (D, PROJ), ((0, 64), (1, 4)), -0.2, 0.2)), 9.99999993922529e-09, 9.999999974752427e-07)
    out_master = scatter_about(splits[7], (INNER, D), INNER ** -0.5, 0.15625, ((0, 4), (1, 64)), jnp.float32)
    out_first = scatter_about(splits[8], (INNER, D), 0.0005, 0.0029296875, ((0, 4), (1, 64)), jnp.float32)
    out_second = jnp.clip(jnp.exp(math.log(9.999999974752427e-07) - 4.6051702 * jax.random.uniform(splits[9], (INNER, D), jnp.float32) ** steps_of(splits[9], (INNER, D), ((0, 4), (1, 64)), -0.2, 0.2)), 9.99999993922529e-09, 9.999999974752427e-07)
    conv_grads = draw_conv_grads(jax.random.fold_in(splits[22], 71), 0)
    conv_master = scatter_about(splits[11], (KCONV + 1, CONV), KCONV ** -0.5, 3.0, ((1, 4),), jnp.float32)
    conv_first = scatter_about(splits[12], (KCONV + 1, CONV), 0.0005, 0.0029296875, ((1, 4),), jnp.float32)
    conv_second = jnp.clip(jnp.exp(math.log(0.01) - 9.2103404 * jax.random.uniform(splits[13], (KCONV + 1, CONV), jnp.float32) ** steps_of(splits[13], (KCONV + 1, CONV), ((1, 4),), -0.2, 0.2)), 9.999999974752427e-07, 0.01)
    head_grads = draw_head_grads(jax.random.fold_in(splits[22], 71), 0)
    head_master = jnp.clip(0.5 + 1.5 * jax.random.uniform(splits[15], (HEADS, HEADDIM + 3), jnp.float32) ** steps_of(splits[15], (HEADS, HEADDIM + 3), ((0, 4),), -0.2, 0.2), 0.5, 2.0)
    head_first = scatter_about(splits[16], (HEADS, HEADDIM + 3), 0.0005, 0.0029296875, ((0, 4),), jnp.float32)
    head_second = jnp.clip(jnp.exp(math.log(0.01) - 9.2103404 * jax.random.uniform(splits[17], (HEADS, HEADDIM + 3), jnp.float32) ** steps_of(splits[17], (HEADS, HEADDIM + 3), ((0, 4),), -0.2, 0.2)), 9.999999974752427e-07, 0.01)
    gain_grads = draw_gain_grads(jax.random.fold_in(splits[22], 71), 0)
    gain_master = jnp.clip(1.0 + 0.1 * jax.random.normal(splits[19], (D,), jnp.float32), 0.5, 1.5)
    gain_first = scatter_about(splits[20], (D,), 0.0005, 0.0029296875, (), jnp.float32)
    gain_second = jnp.clip(jnp.exp(jax.random.uniform(splits[21], (D,), jnp.float32, math.log(9.999999974752427e-07), math.log(0.01))), 9.999999974752427e-07, 0.01)
    return {"acts": acts, "proj_cotangent": proj_cotangent, "inner_acts": inner_acts, "out_cotangent": out_cotangent, "in_master": in_master, "in_first": in_first, "in_second": in_second, "out_master": out_master, "out_first": out_first, "out_second": out_second, "conv_grads": conv_grads, "conv_master": conv_master, "conv_first": conv_first, "conv_second": conv_second, "head_grads": head_grads, "head_master": head_master, "head_first": head_first, "head_second": head_second, "gain_grads": gain_grads, "gain_master": gain_master, "gain_first": gain_first, "gain_second": gain_second}


beta_one = 0.9
beta_two = 0.95
adam_step = 10
adam_eps = 1e-08
learn_rate = 0.003
max_norm = 1.0

def contract(left, right):
    return lax.dot_general(left, right, (((0,), (0,)), ((), ())), preferred_element_type=jnp.float32)

def adam_update(gradient, master, first, second, decay):
    first_new = beta_one * first + (1.0 - beta_one) * gradient
    second_new = beta_two * second + (1.0 - beta_two) * gradient * gradient
    ratio = first_new / (1.0 - beta_one ** adam_step) / (jnp.sqrt(second_new / (1.0 - beta_two ** adam_step)) + adam_eps)
    return (master - learn_rate * (ratio + decay * master), first_new, second_new)

def reference(acts, proj_cotangent, inner_acts, out_cotangent, in_master, in_first, in_second, out_master, out_first, out_second, conv_grads, conv_master, conv_first, conv_second, head_grads, head_master, head_first, head_second, gain_grads, gain_master, gain_first, gain_second):
    grad_in = contract(acts, proj_cotangent)
    grad_out = contract(inner_acts, out_cotangent)
    grad_conv = lax.optimization_barrier(jnp.sum(conv_grads, axis=(0, 1)))
    grad_head = lax.optimization_barrier(jnp.sum(head_grads, axis=(0, 1)))
    grad_gain = lax.optimization_barrier(jnp.sum(gain_grads, axis=(0, 1, 2)))
    squares = jnp.sum(grad_in * grad_in) + jnp.sum(grad_out * grad_out) + jnp.sum(grad_conv * grad_conv) + jnp.sum(grad_head * grad_head) + jnp.sum(grad_gain * grad_gain)
    clip_factor = jnp.minimum(1.0, max_norm / (jnp.sqrt(squares) + 1e-06))
    new_in = adam_update(clip_factor * grad_in, in_master, in_first, in_second, 0.1)
    new_out = adam_update(clip_factor * grad_out, out_master, out_first, out_second, 0.1)
    new_conv = adam_update(clip_factor * grad_conv, conv_master, conv_first, conv_second, 0.1)
    new_head = adam_update(clip_factor * grad_head, head_master, head_first, head_second, 0.0)
    new_gain = adam_update(clip_factor * grad_gain, gain_master, gain_first, gain_second, 0.0)
    return (new_in[0], new_in[1], new_in[2], new_in[0].astype(jnp.bfloat16), new_out[0], new_out[1], new_out[2], new_out[0].astype(jnp.bfloat16), new_conv[0], new_conv[1], new_conv[2], new_head[0], new_head[1], new_head[2], new_gain[0], new_gain[1], new_gain[2])
```

```python
import jax
import jax.numpy as jnp
from jax import lax
from jax.sharding import PartitionSpec as P

beta_one = 0.9
beta_two = 0.95
adam_step = 10
adam_eps = 1e-08
learn_rate = 0.003
max_norm = 1.0


def contract(left, right):
    return lax.dot_general(
        left, right, (((0,), (0,)), ((), ())), preferred_element_type=jnp.float32
    )


def adam_update(gradient, master, first, second, decay):
    first_new = beta_one * first + (1.0 - beta_one) * gradient
    second_new = beta_two * second + (1.0 - beta_two) * gradient * gradient
    ratio = (
        first_new
        / (1.0 - beta_one**adam_step)
        / (jnp.sqrt(second_new / (1.0 - beta_two**adam_step)) + adam_eps)
    )
    return (master - learn_rate * (ratio + decay * master), first_new, second_new)


def body(
    acts,
    proj_cotangent,
    inner_acts,
    out_cotangent,
    in_master,
    in_first,
    in_second,
    out_master,
    out_first,
    out_second,
    conv_grads,
    conv_master,
    conv_first,
    conv_second,
    head_grads,
    head_master,
    head_first,
    head_second,
    gain_grads,
    gain_master,
    gain_first,
    gain_second,
):
    n_dp = lax.axis_size("dp")
    width, n_in = acts.shape[1], proj_cotangent.shape[1]
    rows = width // n_dp
    part_in = contract(acts, proj_cotangent)
    part_out = contract(out_cotangent, inner_acts)
    both = jnp.concatenate([part_in, part_out], axis=1)
    cols = both.shape[1]
    both = both.reshape(n_dp, rows, cols)
    grad_both = lax.psum_scatter(both, "dp", scatter_dimension=0, tiled=True)[0]
    grad_in = grad_both[:, :n_in]
    grad_out_t = grad_both[:, n_in:]

    conv_local = jnp.sum(conv_grads, axis=(0, 1))
    head_local = jnp.sum(head_grads, axis=(0, 1))
    gain_local = jnp.sum(gain_grads, axis=(0, 1, 2))
    n_conv, n_head = conv_local.size, head_local.size
    small = jnp.concatenate(
        [conv_local.reshape(-1), head_local.reshape(-1), gain_local]
    )
    small = lax.psum(small, "dp")
    grad_conv = small[:n_conv].reshape(conv_local.shape)
    grad_head = small[n_conv : n_conv + n_head].reshape(head_local.shape)
    gain_dp = small[n_conv + n_head :]

    data_first = lax.axis_index("dp") == 0
    local_squares = jnp.sum(grad_in * grad_in) + jnp.sum(grad_out_t * grad_out_t)
    dp_squares = lax.psum(local_squares, "dp")
    col_squares = dp_squares + jnp.sum(grad_conv * grad_conv) + jnp.sum(grad_head * grad_head)
    tail = lax.psum(jnp.concatenate([gain_dp, col_squares[None]]), "mp")
    grad_gain = tail[:-1]
    squares = tail[-1] + jnp.sum(grad_gain * grad_gain)
    clip_factor = jnp.minimum(1.0, max_norm / (jnp.sqrt(squares) + 1e-06))

    new_in = adam_update(clip_factor * grad_in, in_master, in_first, in_second, 0.1)
    new_out = adam_update(clip_factor * grad_out_t.T, out_master, out_first, out_second, 0.1)
    new_conv = adam_update(clip_factor * grad_conv, conv_master, conv_first, conv_second, 0.1)
    new_head = adam_update(clip_factor * grad_head, head_master, head_first, head_second, 0.0)
    new_gain = adam_update(clip_factor * grad_gain, gain_master, gain_first, gain_second, 0.0)

    low = jnp.concatenate(
        [new_in[0].astype(jnp.bfloat16), new_out[0].T.astype(jnp.bfloat16)], axis=1
    )
    gathered = lax.all_gather(low, "dp", axis=0, tiled=True)
    in_weights = gathered[:, :n_in]
    out_weights = gathered[:, n_in:].T
    return (
        new_in[0],
        new_in[1],
        new_in[2],
        in_weights,
        new_out[0],
        new_out[1],
        new_out[2],
        out_weights,
        new_conv[0],
        new_conv[1],
        new_conv[2],
        new_head[0],
        new_head[1],
        new_head[2],
        new_gain[0],
        new_gain[1],
        new_gain[2],
    )


def solution(mesh):
    return jax.shard_map(
        body,
        mesh=mesh,
        in_specs=(
            P("dp", None),
            P("dp", "mp"),
            P("dp", "mp"),
            P("dp", None),
            P("dp", "mp"),
            P("dp", "mp"),
            P("dp", "mp"),
            P("mp", "dp"),
            P("mp", "dp"),
            P("mp", "dp"),
            P("dp", None, None, "mp"),
            P(None, "mp"),
            P(None, "mp"),
            P(None, "mp"),
            P("dp", None, "mp", None),
            P("mp", None),
            P("mp", None),
            P("mp", None),
            P("dp", None, "mp", None),
            P(),
            P(),
            P(),
        ),
        out_specs=(
            P("dp", "mp"),
            P("dp", "mp"),
            P("dp", "mp"),
            P(None, "mp"),
            P("mp", "dp"),
            P("mp", "dp"),
            P("mp", "dp"),
            P("mp", None),
            P(None, "mp"),
            P(None, "mp"),
            P(None, "mp"),
            P("mp", None),
            P("mp", None),
            P("mp", None),
            P(),
            P(),
            P(),
        ),
        check_vma=False,
    )
```

```python
import jax
import jax.numpy as jnp
from jax import lax
from jax.sharding import Mesh, PartitionSpec as P

beta_one = 0.9
beta_two = 0.95
adam_step = 10
adam_eps = 1e-08
learn_rate = 0.003
max_norm = 1.0


def contract(left, right):
    return lax.dot_general(
        left, right, (((0,), (0,)), ((), ())), preferred_element_type=jnp.float32
    )


def adam_update(gradient, master, first, second, decay):
    first_new = beta_one * first + (1.0 - beta_one) * gradient
    second_new = beta_two * second + (1.0 - beta_two) * gradient * gradient
    ratio = (
        first_new
        / (1.0 - beta_one**adam_step)
        / (jnp.sqrt(second_new / (1.0 - beta_two**adam_step)) + adam_eps)
    )
    return (master - learn_rate * (ratio + decay * master), first_new, second_new)


DP = ("z", "y", "c")


def nested_psum(value, axes):
    for axis in reversed(axes):
        value = lax.psum(value, axis)
    return value


def body(
    acts,
    proj_cotangent,
    inner_acts,
    out_cotangent,
    in_master,
    in_first,
    in_second,
    out_master,
    out_first,
    out_second,
    conv_grads,
    conv_master,
    conv_first,
    conv_second,
    head_grads,
    head_master,
    head_first,
    head_second,
    gain_grads,
    gain_master,
    gain_first,
    gain_second,
):
    n_dp = lax.axis_size(DP)
    width, n_in = acts.shape[1], proj_cotangent.shape[1]
    rows = width // n_dp
    part_in = contract(acts, proj_cotangent)
    part_out = contract(out_cotangent, inner_acts)
    both = jnp.concatenate([part_in, part_out], axis=1)
    cols = both.shape[1]
    both = both.reshape(n_dp, rows, cols)
    grad_both = lax.psum_scatter(both, DP, scatter_dimension=0, tiled=True)[0]
    grad_in = grad_both[:, :n_in]
    grad_out_t = grad_both[:, n_in:]

    conv_local = jnp.sum(conv_grads, axis=(0, 1))
    head_local = jnp.sum(head_grads, axis=(0, 1))
    gain_local = jnp.sum(gain_grads, axis=(0, 1, 2))
    n_conv, n_head = conv_local.size, head_local.size
    small = jnp.concatenate(
        [conv_local.reshape(-1), head_local.reshape(-1), gain_local]
    )
    small = nested_psum(small, DP)
    grad_conv = small[:n_conv].reshape(conv_local.shape)
    grad_head = small[n_conv : n_conv + n_head].reshape(head_local.shape)
    gain_dp = small[n_conv + n_head :]

    data_first = lax.axis_index(DP) == 0
    local_squares = jnp.sum(grad_in * grad_in) + jnp.sum(grad_out_t * grad_out_t)
    local_squares = local_squares + jnp.where(
        data_first, jnp.sum(grad_conv * grad_conv) + jnp.sum(grad_head * grad_head), 0.0
    )
    col_squares = nested_psum(local_squares, DP)
    tail = lax.psum(jnp.concatenate([gain_dp, col_squares[None]]), "mp")
    grad_gain = tail[:-1]
    squares = tail[-1] + jnp.sum(grad_gain * grad_gain)
    clip_factor = jnp.minimum(1.0, max_norm / (jnp.sqrt(squares) + 1e-06))

    new_in = adam_update(clip_factor * grad_in, in_master, in_first, in_second, 0.1)
    new_out = adam_update(clip_factor * grad_out_t.T, out_master, out_first, out_second, 0.1)
    new_conv = adam_update(clip_factor * grad_conv, conv_master, conv_first, conv_second, 0.1)
    new_head = adam_update(clip_factor * grad_head, head_master, head_first, head_second, 0.0)
    new_gain = adam_update(clip_factor * grad_gain, gain_master, gain_first, gain_second, 0.0)

    low = jnp.concatenate(
        [new_in[0].astype(jnp.bfloat16), new_out[0].T.astype(jnp.bfloat16)], axis=1
    )
    gathered = lax.all_gather(low, DP, axis=0, tiled=True)
    in_weights = gathered[:, :n_in]
    out_weights = gathered[:, n_in:].T
    return (
        new_in[0],
        new_in[1],
        new_in[2],
        in_weights,
        new_out[0],
        new_out[1],
        new_out[2],
        out_weights,
        new_conv[0],
        new_conv[1],
        new_conv[2],
        new_head[0],
        new_head[1],
        new_head[2],
        new_gain[0],
        new_gain[1],
        new_gain[2],
    )


def solution(mesh):
    n_dp, n_mp = mesh.devices.shape
    split = Mesh(mesh.devices.reshape(n_dp // 8, 4, 2, n_mp), DP + ("mp",))
    return jax.shard_map(
        body,
        mesh=split,
        in_specs=(
            P(DP, None),
            P(DP, "mp"),
            P(DP, "mp"),
            P(DP, None),
            P(DP, "mp"),
            P(DP, "mp"),
            P(DP, "mp"),
            P("mp", DP),
            P("mp", DP),
            P("mp", DP),
            P(DP, None, None, "mp"),
            P(None, "mp"),
            P(None, "mp"),
            P(None, "mp"),
            P(DP, None, "mp", None),
            P("mp", None),
            P("mp", None),
            P("mp", None),
            P(DP, None, "mp", None),
            P(),
            P(),
            P(),
        ),
        out_specs=(
            P(DP, "mp"),
            P(DP, "mp"),
            P(DP, "mp"),
            P(None, "mp"),
            P("mp", DP),
            P("mp", DP),
            P("mp", DP),
            P("mp", None),
            P(None, "mp"),
            P(None, "mp"),
            P(None, "mp"),
            P("mp", None),
            P("mp", None),
            P("mp", None),
            P(),
            P(),
            P(),
        ),
        check_vma=False,
    )
```

```python
import jax
import jax.numpy as jnp
from jax import lax
from jax.sharding import Mesh, PartitionSpec as P

beta_one = 0.9
beta_two = 0.95
adam_step = 10
adam_eps = 1e-08
learn_rate = 0.003
max_norm = 1.0


def contract(left, right):
    return lax.dot_general(
        left, right, (((0,), (0,)), ((), ())), preferred_element_type=jnp.float32
    )


def adam_update(gradient, master, first, second, decay):
    first_new = beta_one * first + (1.0 - beta_one) * gradient
    second_new = beta_two * second + (1.0 - beta_two) * gradient * gradient
    ratio = (
        first_new
        / (1.0 - beta_one**adam_step)
        / (jnp.sqrt(second_new / (1.0 - beta_two**adam_step)) + adam_eps)
    )
    return (master - learn_rate * (ratio + decay * master), first_new, second_new)


DP = ("z", "y", "c")


def nested_psum(value, axes):
    for axis in reversed(axes):
        value = lax.psum(value, axis)
    return value


def scatter_sum(value, axis):
    n = lax.axis_size(axis)
    me = lax.axis_index(axis)
    total = lax.dynamic_index_in_dim(value, me, 0, keepdims=False)
    for shift in range(1, n):
        part = lax.dynamic_index_in_dim(value, (me + shift) % n, 0, keepdims=False)
        pairs = [(j, (j + shift) % n) for j in range(n)]
        total = total + lax.ppermute(part, axis, pairs)
    return total


def body(
    acts,
    proj_cotangent,
    inner_acts,
    out_cotangent,
    in_master,
    in_first,
    in_second,
    out_master,
    out_first,
    out_second,
    conv_grads,
    conv_master,
    conv_first,
    conv_second,
    head_grads,
    head_master,
    head_first,
    head_second,
    gain_grads,
    gain_master,
    gain_first,
    gain_second,
):
    n_dp = lax.axis_size(DP)
    width, n_in = acts.shape[1], proj_cotangent.shape[1]
    rows = width // n_dp
    part_in = contract(acts, proj_cotangent)
    part_out = contract(out_cotangent, inner_acts)
    sizes = [lax.axis_size(a) for a in DP]
    both = jnp.concatenate(
        [part_in.reshape(*sizes, rows, -1), part_out.reshape(*sizes, rows, -1)], axis=-1
    )
    both = jnp.moveaxis(both, 2, 0)
    both = scatter_sum(both, DP[2])
    both = jnp.moveaxis(both, 1, 0)
    both = scatter_sum(both, DP[1])
    grad_both = scatter_sum(both, DP[0])
    grad_in = grad_both[:, :n_in]
    grad_out_t = grad_both[:, n_in:]

    conv_local = jnp.sum(conv_grads, axis=(0, 1))
    head_local = jnp.sum(head_grads, axis=(0, 1))
    gain_local = jnp.sum(gain_grads, axis=(0, 1, 2))
    n_conv, n_head = conv_local.size, head_local.size
    small = jnp.concatenate(
        [conv_local.reshape(-1), head_local.reshape(-1), gain_local]
    )
    small = nested_psum(small, DP)
    grad_conv = small[:n_conv].reshape(conv_local.shape)
    grad_head = small[n_conv : n_conv + n_head].reshape(head_local.shape)
    gain_dp = small[n_conv + n_head :]

    data_first = lax.axis_index(DP) == 0
    local_squares = jnp.sum(grad_in * grad_in) + jnp.sum(grad_out_t * grad_out_t)
    local_squares = local_squares + jnp.where(
        data_first, jnp.sum(grad_conv * grad_conv) + jnp.sum(grad_head * grad_head), 0.0
    )
    col_squares = nested_psum(local_squares, DP)
    tail = lax.psum(jnp.concatenate([gain_dp, col_squares[None]]), "mp")
    grad_gain = tail[:-1]
    squares = tail[-1] + jnp.sum(grad_gain * grad_gain)
    clip_factor = jnp.minimum(1.0, max_norm / (jnp.sqrt(squares) + 1e-06))

    new_in = adam_update(clip_factor * grad_in, in_master, in_first, in_second, 0.1)
    new_out = adam_update(clip_factor * grad_out_t.T, out_master, out_first, out_second, 0.1)
    new_conv = adam_update(clip_factor * grad_conv, conv_master, conv_first, conv_second, 0.1)
    new_head = adam_update(clip_factor * grad_head, head_master, head_first, head_second, 0.0)
    new_gain = adam_update(clip_factor * grad_gain, gain_master, gain_first, gain_second, 0.0)

    low = jnp.concatenate(
        [new_in[0].astype(jnp.bfloat16), new_out[0].T.astype(jnp.bfloat16)], axis=1
    )
    gathered = lax.all_gather(low, DP, axis=0, tiled=True)
    in_weights = gathered[:, :n_in]
    out_weights = gathered[:, n_in:].T
    return (
        new_in[0],
        new_in[1],
        new_in[2],
        in_weights,
        new_out[0],
        new_out[1],
        new_out[2],
        out_weights,
        new_conv[0],
        new_conv[1],
        new_conv[2],
        new_head[0],
        new_head[1],
        new_head[2],
        new_gain[0],
        new_gain[1],
        new_gain[2],
    )


def solution(mesh):
    n_dp, n_mp = mesh.devices.shape
    split = Mesh(mesh.devices.reshape(n_dp // 8, 4, 2, n_mp), DP + ("mp",))
    return jax.shard_map(
        body,
        mesh=split,
        in_specs=(
            P(DP, None),
            P(DP, "mp"),
            P(DP, "mp"),
            P(DP, None),
            P(DP, "mp"),
            P(DP, "mp"),
            P(DP, "mp"),
            P("mp", DP),
            P("mp", DP),
            P("mp", DP),
            P(DP, None, None, "mp"),
            P(None, "mp"),
            P(None, "mp"),
            P(None, "mp"),
            P(DP, None, "mp", None),
            P("mp", None),
            P("mp", None),
            P("mp", None),
            P(DP, None, "mp", None),
            P(),
            P(),
            P(),
        ),
        out_specs=(
            P(DP, "mp"),
            P(DP, "mp"),
            P(DP, "mp"),
            P(None, "mp"),
            P("mp", DP),
            P("mp", DP),
            P("mp", DP),
            P("mp", None),
            P(None, "mp"),
            P(None, "mp"),
            P(None, "mp"),
            P("mp", None),
            P("mp", None),
            P("mp", None),
            P(),
            P(),
            P(),
        ),
        check_vma=False,
    )
```

```python
import jax
import jax.numpy as jnp
from jax import lax
from jax.sharding import Mesh, PartitionSpec as P

beta_one = 0.9
beta_two = 0.95
adam_step = 10
adam_eps = 1e-08
learn_rate = 0.003
max_norm = 1.0


def contract(left, right):
    return lax.dot_general(
        left, right, (((0,), (0,)), ((), ())), preferred_element_type=jnp.float32
    )


def adam_update(gradient, master, first, second, decay):
    first_new = beta_one * first + (1.0 - beta_one) * gradient
    second_new = beta_two * second + (1.0 - beta_two) * gradient * gradient
    ratio = (
        first_new
        / (1.0 - beta_one**adam_step)
        / (jnp.sqrt(second_new / (1.0 - beta_two**adam_step)) + adam_eps)
    )
    return (master - learn_rate * (ratio + decay * master), first_new, second_new)


DP = ("z", "y", "c")


def nested_psum(value, axes):
    for axis in reversed(axes):
        value = lax.psum(value, axis)
    return value


def scatter_sum(value, small, axis):
    n = lax.axis_size(axis)
    me = lax.axis_index(axis)
    total = lax.dynamic_index_in_dim(value, me, 0, keepdims=False)
    small_total = small
    for shift in range(1, n):
        part = lax.dynamic_index_in_dim(value, (me + shift) % n, 0, keepdims=False)
        pairs = [(j, (j + shift) % n) for j in range(n)]
        got, got_small = lax.ppermute((part, small), axis, pairs)
        total = total + got
        small_total = small_total + got_small
    return total, small_total


def gather_stack(value, axis):
    n = lax.axis_size(axis)
    me = lax.axis_index(axis)
    pieces = [value]
    for shift in range(1, n):
        pairs = [(j, (j + shift) % n) for j in range(n)]
        pieces.append(lax.ppermute(value, axis, pairs))
    stacked = jnp.stack(pieces[::-1])
    return jnp.roll(stacked, me + 1, axis=0)


def body(
    acts,
    proj_cotangent,
    inner_acts,
    out_cotangent,
    in_master,
    in_first,
    in_second,
    out_master,
    out_first,
    out_second,
    conv_grads,
    conv_master,
    conv_first,
    conv_second,
    head_grads,
    head_master,
    head_first,
    head_second,
    gain_grads,
    gain_master,
    gain_first,
    gain_second,
):
    n_dp = lax.axis_size(DP)
    width, n_in = acts.shape[1], proj_cotangent.shape[1]
    rows = width // n_dp
    part_in = contract(acts, proj_cotangent)
    part_out = contract(out_cotangent, inner_acts)
    sizes = [lax.axis_size(a) for a in DP]
    both = jnp.concatenate(
        [part_in.reshape(*sizes, rows, -1), part_out.reshape(*sizes, rows, -1)], axis=-1
    )
    conv_local = jnp.sum(conv_grads, axis=(0, 1))
    head_local = jnp.sum(head_grads, axis=(0, 1))
    gain_local = jnp.sum(gain_grads, axis=(0, 1, 2))
    n_conv, n_head = conv_local.size, head_local.size
    small = jnp.concatenate(
        [conv_local.reshape(-1), head_local.reshape(-1), gain_local]
    )
    both = jnp.moveaxis(both, 2, 0)
    both, small = scatter_sum(both, small, DP[2])
    both = jnp.moveaxis(both, 1, 0)
    both, small = scatter_sum(both, small, DP[1])
    grad_both, small = scatter_sum(both, small, DP[0])
    grad_in = grad_both[:, :n_in]
    grad_out_t = grad_both[:, n_in:]

    grad_conv = small[:n_conv].reshape(conv_local.shape)
    grad_head = small[n_conv : n_conv + n_head].reshape(head_local.shape)
    gain_dp = small[n_conv + n_head :]

    data_first = lax.axis_index(DP) == 0
    local_squares = jnp.sum(grad_in * grad_in) + jnp.sum(grad_out_t * grad_out_t)
    local_squares = local_squares + jnp.where(
        data_first, jnp.sum(grad_conv * grad_conv) + jnp.sum(grad_head * grad_head), 0.0
    )
    col_squares = nested_psum(local_squares, DP)
    tail = lax.psum(jnp.concatenate([gain_dp, col_squares[None]]), "mp")
    grad_gain = tail[:-1]
    squares = tail[-1] + jnp.sum(grad_gain * grad_gain)
    clip_factor = jnp.minimum(1.0, max_norm / (jnp.sqrt(squares) + 1e-06))

    new_in = adam_update(clip_factor * grad_in, in_master, in_first, in_second, 0.1)
    new_out = adam_update(clip_factor * grad_out_t.T, out_master, out_first, out_second, 0.1)
    new_conv = adam_update(clip_factor * grad_conv, conv_master, conv_first, conv_second, 0.1)
    new_head = adam_update(clip_factor * grad_head, head_master, head_first, head_second, 0.0)
    new_gain = adam_update(clip_factor * grad_gain, gain_master, gain_first, gain_second, 0.0)

    low = jnp.concatenate(
        [new_in[0].astype(jnp.bfloat16), new_out[0].T.astype(jnp.bfloat16)], axis=1
    )
    for axis in DP:
        low = gather_stack(low, axis)
    gathered = jnp.transpose(low, (2, 1, 0, 3, 4)).reshape(-1, low.shape[-1])
    in_weights = gathered[:, :n_in]
    out_weights = gathered[:, n_in:].T
    return (
        new_in[0],
        new_in[1],
        new_in[2],
        in_weights,
        new_out[0],
        new_out[1],
        new_out[2],
        out_weights,
        new_conv[0],
        new_conv[1],
        new_conv[2],
        new_head[0],
        new_head[1],
        new_head[2],
        new_gain[0],
        new_gain[1],
        new_gain[2],
    )


def solution(mesh):
    n_dp, n_mp = mesh.devices.shape
    split = Mesh(mesh.devices.reshape(n_dp // 8, 4, 2, n_mp), DP + ("mp",))
    return jax.shard_map(
        body,
        mesh=split,
        in_specs=(
            P(DP, None),
            P(DP, "mp"),
            P(DP, "mp"),
            P(DP, None),
            P(DP, "mp"),
            P(DP, "mp"),
            P(DP, "mp"),
            P("mp", DP),
            P("mp", DP),
            P("mp", DP),
            P(DP, None, None, "mp"),
            P(None, "mp"),
            P(None, "mp"),
            P(None, "mp"),
            P(DP, None, "mp", None),
            P("mp", None),
            P("mp", None),
            P("mp", None),
            P(DP, None, "mp", None),
            P(),
            P(),
            P(),
        ),
        out_specs=(
            P(DP, "mp"),
            P(DP, "mp"),
            P(DP, "mp"),
            P(None, "mp"),
            P("mp", DP),
            P("mp", DP),
            P("mp", DP),
            P("mp", None),
            P(None, "mp"),
            P(None, "mp"),
            P(None, "mp"),
            P("mp", None),
            P("mp", None),
            P("mp", None),
            P(),
            P(),
            P(),
        ),
        check_vma=False,
    )
```

```python
import jax
import jax.numpy as jnp
from jax import lax
from jax.sharding import Mesh, PartitionSpec as P

beta_one = 0.9
beta_two = 0.95
adam_step = 10
adam_eps = 1e-08
learn_rate = 0.003
max_norm = 1.0


def contract(left, right):
    return lax.dot_general(
        left, right, (((0,), (0,)), ((), ())), preferred_element_type=jnp.float32
    )


def adam_update(gradient, master, first, second, decay):
    first_new = beta_one * first + (1.0 - beta_one) * gradient
    second_new = beta_two * second + (1.0 - beta_two) * gradient * gradient
    ratio = (
        first_new
        / (1.0 - beta_one**adam_step)
        / (jnp.sqrt(second_new / (1.0 - beta_two**adam_step)) + adam_eps)
    )
    return (master - learn_rate * (ratio + decay * master), first_new, second_new)


DP = ("z", "y", "c")


def nested_psum(value, axes):
    for axis in reversed(axes):
        value = lax.psum(value, axis)
    return value


def by_source(pieces, me):
    stacked = jnp.stack(pieces[::-1])
    return jnp.roll(stacked, me + 1, axis=0)


def scatter_sum(value, rows, axis):
    n = lax.axis_size(axis)
    me = lax.axis_index(axis)
    lead = (0,) * (value.ndim - 3)
    total = lax.dynamic_index_in_dim(value, me, 0, keepdims=False)
    smalls = [total[lead][rows:]]
    for shift in range(1, n):
        part = lax.dynamic_index_in_dim(value, (me + shift) % n, 0, keepdims=False)
        pairs = [(j, (j + shift) % n) for j in range(n)]
        got = lax.ppermute(part, axis, pairs)
        total = total + got
        smalls.append(got[lead][rows:])
    small = jnp.sum(by_source(smalls, me), axis=0)
    grad = total[..., :rows, :]
    small = jnp.broadcast_to(small, grad.shape[:-2] + small.shape)
    return jnp.concatenate([grad, small], axis=-2)


def butterfly_sum(value, axis):
    n = lax.axis_size(axis)
    step = 1
    while step < n:
        pairs = [(j, j ^ step) for j in range(n)]
        value = value + lax.ppermute(value, axis, pairs)
        step *= 2
    return value


def gather_stack(value, axis):
    n = lax.axis_size(axis)
    me = lax.axis_index(axis)
    pieces = [value]
    for shift in range(1, n):
        pairs = [(j, (j + shift) % n) for j in range(n)]
        pieces.append(lax.ppermute(value, axis, pairs))
    stacked = jnp.stack(pieces[::-1])
    return jnp.roll(stacked, me + 1, axis=0)


def body(
    acts,
    proj_cotangent,
    inner_acts,
    out_cotangent,
    in_master,
    in_first,
    in_second,
    out_master,
    out_first,
    out_second,
    conv_grads,
    conv_master,
    conv_first,
    conv_second,
    head_grads,
    head_master,
    head_first,
    head_second,
    gain_grads,
    gain_master,
    gain_first,
    gain_second,
):
    n_dp = lax.axis_size(DP)
    width, n_in = acts.shape[1], proj_cotangent.shape[1]
    rows = width // n_dp
    part_in = contract(acts, proj_cotangent)
    part_out = contract(out_cotangent, inner_acts)
    sizes = [lax.axis_size(a) for a in DP]
    both = jnp.concatenate(
        [part_in.reshape(*sizes, rows, -1), part_out.reshape(*sizes, rows, -1)], axis=-1
    )
    cols = both.shape[-1]
    conv_local = jnp.sum(conv_grads, axis=(0, 1))
    head_local = jnp.sum(head_grads, axis=(0, 1))
    gain_local = jnp.sum(gain_grads, axis=(0, 1, 2))
    n_conv, n_head = conv_local.size, head_local.size
    small = jnp.concatenate(
        [conv_local.reshape(-1), head_local.reshape(-1), gain_local]
    )
    n_small = small.size
    small_rows = -(-n_small // cols)
    small = jnp.pad(small, (0, small_rows * cols - n_small)).reshape(small_rows, cols)
    both = jnp.concatenate(
        [both, jnp.broadcast_to(small, both.shape[:-2] + small.shape)], axis=-2
    )
    both = jnp.moveaxis(both, 2, 0)
    both = scatter_sum(both, rows, DP[2])
    both = jnp.moveaxis(both, 1, 0)
    both = scatter_sum(both, rows, DP[1])
    both = scatter_sum(both, rows, DP[0])
    grad_both = both[:rows]
    small = both[rows:].reshape(-1)[:n_small]
    grad_in = grad_both[:, :n_in]
    grad_out_t = grad_both[:, n_in:]

    grad_conv = small[:n_conv].reshape(conv_local.shape)
    grad_head = small[n_conv : n_conv + n_head].reshape(head_local.shape)
    gain_dp = small[n_conv + n_head :]

    data_first = lax.axis_index(DP) == 0
    local_squares = jnp.sum(grad_in * grad_in) + jnp.sum(grad_out_t * grad_out_t)
    local_squares = local_squares + jnp.where(
        data_first, jnp.sum(grad_conv * grad_conv) + jnp.sum(grad_head * grad_head), 0.0
    )
    col_squares = local_squares
    for axis in reversed(DP):
        col_squares = butterfly_sum(col_squares, axis)
    tail = butterfly_sum(jnp.concatenate([gain_dp, col_squares[None]]), "mp")
    grad_gain = tail[:-1]
    squares = tail[-1] + jnp.sum(grad_gain * grad_gain)
    clip_factor = jnp.minimum(1.0, max_norm / (jnp.sqrt(squares) + 1e-06))

    new_in = adam_update(clip_factor * grad_in, in_master, in_first, in_second, 0.1)
    new_out = adam_update(clip_factor * grad_out_t.T, out_master, out_first, out_second, 0.1)
    new_conv = adam_update(clip_factor * grad_conv, conv_master, conv_first, conv_second, 0.1)
    new_head = adam_update(clip_factor * grad_head, head_master, head_first, head_second, 0.0)
    new_gain = adam_update(clip_factor * grad_gain, gain_master, gain_first, gain_second, 0.0)

    low = jnp.concatenate(
        [new_in[0].astype(jnp.bfloat16), new_out[0].T.astype(jnp.bfloat16)], axis=1
    )
    for axis in DP:
        low = gather_stack(low, axis)
    gathered = jnp.transpose(low, (2, 1, 0, 3, 4)).reshape(-1, low.shape[-1])
    in_weights = gathered[:, :n_in]
    out_weights = gathered[:, n_in:].T
    return (
        new_in[0],
        new_in[1],
        new_in[2],
        in_weights,
        new_out[0],
        new_out[1],
        new_out[2],
        out_weights,
        new_conv[0],
        new_conv[1],
        new_conv[2],
        new_head[0],
        new_head[1],
        new_head[2],
        new_gain[0],
        new_gain[1],
        new_gain[2],
    )


def solution(mesh):
    n_dp, n_mp = mesh.devices.shape
    split = Mesh(mesh.devices.reshape(n_dp // 8, 4, 2, n_mp), DP + ("mp",))
    return jax.shard_map(
        body,
        mesh=split,
        in_specs=(
            P(DP, None),
            P(DP, "mp"),
            P(DP, "mp"),
            P(DP, None),
            P(DP, "mp"),
            P(DP, "mp"),
            P(DP, "mp"),
            P("mp", DP),
            P("mp", DP),
            P("mp", DP),
            P(DP, None, None, "mp"),
            P(None, "mp"),
            P(None, "mp"),
            P(None, "mp"),
            P(DP, None, "mp", None),
            P("mp", None),
            P("mp", None),
            P("mp", None),
            P(DP, None, "mp", None),
            P(),
            P(),
            P(),
        ),
        out_specs=(
            P(DP, "mp"),
            P(DP, "mp"),
            P(DP, "mp"),
            P(None, "mp"),
            P("mp", DP),
            P("mp", DP),
            P("mp", DP),
            P("mp", None),
            P(None, "mp"),
            P(None, "mp"),
            P(None, "mp"),
            P("mp", None),
            P("mp", None),
            P("mp", None),
            P(),
            P(),
            P(),
        ),
        check_vma=False,
    )
```

```python
import jax
import jax.numpy as jnp
from jax import lax
from jax.sharding import Mesh, PartitionSpec as P

beta_one = 0.9
beta_two = 0.95
adam_step = 10
adam_eps = 1e-08
learn_rate = 0.003
max_norm = 1.0


def contract(left, right):
    return lax.dot_general(
        left, right, (((0,), (0,)), ((), ())), preferred_element_type=jnp.float32
    )


def adam_update(gradient, master, first, second, decay):
    first_new = beta_one * first + (1.0 - beta_one) * gradient
    second_new = beta_two * second + (1.0 - beta_two) * gradient * gradient
    ratio = (
        first_new
        / (1.0 - beta_one**adam_step)
        / (jnp.sqrt(second_new / (1.0 - beta_two**adam_step)) + adam_eps)
    )
    return (master - learn_rate * (ratio + decay * master), first_new, second_new)


DP = ("z", "y", "c")


def nested_psum(value, axes):
    for axis in reversed(axes):
        value = lax.psum(value, axis)
    return value


def by_source(pieces, me):
    stacked = jnp.stack(pieces[::-1])
    return jnp.roll(stacked, me + 1, axis=0)


def scatter_sum(value, rows, axis, dim):
    n = lax.axis_size(axis)
    me = lax.axis_index(axis)
    lead = (0,) * (value.ndim - 3)
    total = lax.dynamic_index_in_dim(value, me, dim, keepdims=False)
    smalls = [total[lead][rows:]]
    for shift in range(1, n):
        part = lax.dynamic_index_in_dim(value, (me + shift) % n, dim, keepdims=False)
        pairs = [(j, (j + shift) % n) for j in range(n)]
        got = lax.ppermute(part, axis, pairs)
        total = total + got
        smalls.append(got[lead][rows:])
    small = jnp.sum(by_source(smalls, me), axis=0)
    grad = total[..., :rows, :]
    small = jnp.broadcast_to(small, grad.shape[:-2] + small.shape)
    return jnp.concatenate([grad, small], axis=-2)


def butterfly_sum(value, axis):
    n = lax.axis_size(axis)
    step = 1
    while step < n:
        pairs = [(j, j ^ step) for j in range(n)]
        value = value + lax.ppermute(value, axis, pairs)
        step *= 2
    return value


def gather_stack(value, axis):
    n = lax.axis_size(axis)
    me = lax.axis_index(axis)
    pieces = [value]
    for shift in range(1, n):
        pairs = [(j, (j + shift) % n) for j in range(n)]
        pieces.append(lax.ppermute(value, axis, pairs))
    stacked = jnp.stack(pieces[::-1])
    return jnp.roll(stacked, me + 1, axis=0)


def body(
    acts,
    proj_cotangent,
    inner_acts,
    out_cotangent,
    in_master,
    in_first,
    in_second,
    out_master,
    out_first,
    out_second,
    conv_grads,
    conv_master,
    conv_first,
    conv_second,
    head_grads,
    head_master,
    head_first,
    head_second,
    gain_grads,
    gain_master,
    gain_first,
    gain_second,
):
    n_dp = lax.axis_size(DP)
    width, n_in = acts.shape[1], proj_cotangent.shape[1]
    rows = width // n_dp
    part_in = contract(acts, proj_cotangent)
    part_out = contract(out_cotangent, inner_acts)
    sizes = [lax.axis_size(a) for a in DP]
    both = jnp.concatenate(
        [part_in.reshape(*sizes, rows, -1), part_out.reshape(*sizes, rows, -1)], axis=-1
    )
    cols = both.shape[-1]
    conv_local = jnp.sum(conv_grads, axis=(0, 1))
    head_local = jnp.sum(head_grads, axis=(0, 1))
    gain_local = jnp.sum(gain_grads, axis=(0, 1, 2))
    n_conv, n_head = conv_local.size, head_local.size
    small = jnp.concatenate(
        [conv_local.reshape(-1), head_local.reshape(-1), gain_local]
    )
    n_small = small.size
    small_rows = -(-n_small // cols)
    small = jnp.pad(small, (0, small_rows * cols - n_small)).reshape(small_rows, cols)
    both = jnp.concatenate(
        [both, jnp.broadcast_to(small, both.shape[:-2] + small.shape)], axis=-2
    )
    both = scatter_sum(both, rows, DP[2], 2)
    both = scatter_sum(both, rows, DP[1], 1)
    both = scatter_sum(both, rows, DP[0], 0)
    grad_both = both[:rows]
    small = both[rows:].reshape(-1)[:n_small]
    grad_in = grad_both[:, :n_in]
    grad_out_t = grad_both[:, n_in:]

    grad_conv = small[:n_conv].reshape(conv_local.shape)
    grad_head = small[n_conv : n_conv + n_head].reshape(head_local.shape)
    gain_dp = small[n_conv + n_head :]

    data_first = lax.axis_index(DP) == 0
    local_squares = jnp.sum(grad_in * grad_in) + jnp.sum(grad_out_t * grad_out_t)
    local_squares = local_squares + jnp.where(
        data_first, jnp.sum(grad_conv * grad_conv) + jnp.sum(grad_head * grad_head), 0.0
    )
    col_squares = local_squares
    for axis in reversed(DP):
        col_squares = butterfly_sum(col_squares, axis)
    tail = butterfly_sum(jnp.concatenate([gain_dp, col_squares[None]]), "mp")
    grad_gain = tail[:-1]
    squares = tail[-1] + jnp.sum(grad_gain * grad_gain)
    clip_factor = jnp.minimum(1.0, max_norm / (jnp.sqrt(squares) + 1e-06))

    new_in = adam_update(clip_factor * grad_in, in_master, in_first, in_second, 0.1)
    new_out = adam_update(clip_factor * grad_out_t.T, out_master, out_first, out_second, 0.1)
    new_conv = adam_update(clip_factor * grad_conv, conv_master, conv_first, conv_second, 0.1)
    new_head = adam_update(clip_factor * grad_head, head_master, head_first, head_second, 0.0)
    new_gain = adam_update(clip_factor * grad_gain, gain_master, gain_first, gain_second, 0.0)

    low = jnp.concatenate(
        [new_in[0].astype(jnp.bfloat16), new_out[0].T.astype(jnp.bfloat16)], axis=1
    )
    for axis in DP:
        low = gather_stack(low, axis)
    in_weights = jnp.transpose(low[..., :n_in], (2, 1, 0, 3, 4)).reshape(-1, n_in)
    out_weights = jnp.transpose(low[..., n_in:], (4, 2, 1, 0, 3)).reshape(cols - n_in, -1)
    return (
        new_in[0],
        new_in[1],
        new_in[2],
        in_weights,
        new_out[0],
        new_out[1],
        new_out[2],
        out_weights,
        new_conv[0],
        new_conv[1],
        new_conv[2],
        new_head[0],
        new_head[1],
        new_head[2],
        new_gain[0],
        new_gain[1],
        new_gain[2],
    )


def solution(mesh):
    n_dp, n_mp = mesh.devices.shape
    split = Mesh(mesh.devices.reshape(n_dp // 8, 4, 2, n_mp), DP + ("mp",))
    return jax.shard_map(
        body,
        mesh=split,
        in_specs=(
            P(DP, None),
            P(DP, "mp"),
            P(DP, "mp"),
            P(DP, None),
            P(DP, "mp"),
            P(DP, "mp"),
            P(DP, "mp"),
            P("mp", DP),
            P("mp", DP),
            P("mp", DP),
            P(DP, None, None, "mp"),
            P(None, "mp"),
            P(None, "mp"),
            P(None, "mp"),
            P(DP, None, "mp", None),
            P("mp", None),
            P("mp", None),
            P("mp", None),
            P(DP, None, "mp", None),
            P(),
            P(),
            P(),
        ),
        out_specs=(
            P(DP, "mp"),
            P(DP, "mp"),
            P(DP, "mp"),
            P(None, "mp"),
            P("mp", DP),
            P("mp", DP),
            P("mp", DP),
            P("mp", None),
            P(None, "mp"),
            P(None, "mp"),
            P(None, "mp"),
            P("mp", None),
            P("mp", None),
            P("mp", None),
            P(),
            P(),
            P(),
        ),
        check_vma=False,
    )
```

```python
import jax
import jax.numpy as jnp
from jax import lax
from jax.sharding import Mesh, PartitionSpec as P

beta_one = 0.9
beta_two = 0.95
adam_step = 10
adam_eps = 1e-08
learn_rate = 0.003
max_norm = 1.0


def contract(left, right):
    return lax.dot_general(
        left, right, (((0,), (0,)), ((), ())), preferred_element_type=jnp.float32
    )


def adam_update(gradient, master, first, second, decay):
    first_new = beta_one * first + (1.0 - beta_one) * gradient
    second_new = beta_two * second + (1.0 - beta_two) * gradient * gradient
    ratio = (
        first_new
        / (1.0 - beta_one**adam_step)
        / (jnp.sqrt(second_new / (1.0 - beta_two**adam_step)) + adam_eps)
    )
    return (master - learn_rate * (ratio + decay * master), first_new, second_new)


DP = ("z", "y", "c")


def nested_psum(value, axes):
    for axis in reversed(axes):
        value = lax.psum(value, axis)
    return value


def by_source(pieces, me):
    stacked = jnp.stack(pieces[::-1])
    return jnp.roll(stacked, me + 1, axis=0)


def scatter_sum(value, rows, axis, dim):
    n = lax.axis_size(axis)
    me = lax.axis_index(axis)
    lead = (0,) * (value.ndim - 3)
    pick = lambda shift: lax.dynamic_index_in_dim(value, (me + shift) % n, dim, keepdims=False)
    shifted = lambda x, shift: lax.ppermute(x, axis, [(j, (j + shift) % n) for j in range(n)])
    total = pick(0)
    smalls = [total[lead][rows:]]
    relay = n == 4 and total.ndim == 3 and total.shape[0] % 2 == 0
    if relay:
        half = total.shape[0] // 2
        far = pick(2)
        got1 = shifted(pick(1), 1)
        got_near = shifted(far[:half], 2)
        got3, passing = shifted((pick(3), far[half:]), 3)
        got_far = jnp.concatenate([got_near, shifted(passing, 3)], axis=0)
        for got in (got1, got_far, got3):
            total = total + got
            smalls.append(got[lead][rows:])
    else:
        for shift in range(1, n):
            got = shifted(pick(shift), shift)
            total = total + got
            smalls.append(got[lead][rows:])
    small = jnp.sum(by_source(smalls, me), axis=0)
    grad = total[..., :rows, :]
    small = jnp.broadcast_to(small, grad.shape[:-2] + small.shape)
    return jnp.concatenate([grad, small], axis=-2)


def butterfly_sum(value, axis):
    n = lax.axis_size(axis)
    step = 1
    while step < n:
        pairs = [(j, j ^ step) for j in range(n)]
        value = value + lax.ppermute(value, axis, pairs)
        step *= 2
    return value


def gather_stack(value, axis):
    n = lax.axis_size(axis)
    me = lax.axis_index(axis)
    pieces = [value]
    for shift in range(1, n):
        pairs = [(j, (j + shift) % n) for j in range(n)]
        pieces.append(lax.ppermute(value, axis, pairs))
    stacked = jnp.stack(pieces[::-1])
    return jnp.roll(stacked, me + 1, axis=0)


def body(
    acts,
    proj_cotangent,
    inner_acts,
    out_cotangent,
    in_master,
    in_first,
    in_second,
    out_master,
    out_first,
    out_second,
    conv_grads,
    conv_master,
    conv_first,
    conv_second,
    head_grads,
    head_master,
    head_first,
    head_second,
    gain_grads,
    gain_master,
    gain_first,
    gain_second,
):
    n_dp = lax.axis_size(DP)
    width, n_in = acts.shape[1], proj_cotangent.shape[1]
    rows = width // n_dp
    part_in = contract(acts, proj_cotangent)
    part_out = contract(out_cotangent, inner_acts)
    sizes = [lax.axis_size(a) for a in DP]
    both = jnp.concatenate(
        [part_in.reshape(*sizes, rows, -1), part_out.reshape(*sizes, rows, -1)], axis=-1
    )
    cols = both.shape[-1]
    conv_local = jnp.sum(conv_grads, axis=(0, 1))
    head_local = jnp.sum(head_grads, axis=(0, 1))
    gain_local = jnp.sum(gain_grads, axis=(0, 1, 2))
    n_conv, n_head = conv_local.size, head_local.size
    small = jnp.concatenate(
        [conv_local.reshape(-1), head_local.reshape(-1), gain_local]
    )
    n_small = small.size
    small_rows = -(-n_small // cols)
    small = jnp.pad(small, (0, small_rows * cols - n_small)).reshape(small_rows, cols)
    both = jnp.concatenate(
        [both, jnp.broadcast_to(small, both.shape[:-2] + small.shape)], axis=-2
    )
    both = scatter_sum(both, rows, DP[2], 2)
    both = scatter_sum(both, rows, DP[1], 1)
    both = scatter_sum(both, rows, DP[0], 0)
    grad_both = both[:rows]
    small = both[rows:].reshape(-1)[:n_small]
    grad_in = grad_both[:, :n_in]
    grad_out_t = grad_both[:, n_in:]

    grad_conv = small[:n_conv].reshape(conv_local.shape)
    grad_head = small[n_conv : n_conv + n_head].reshape(head_local.shape)
    gain_dp = small[n_conv + n_head :]

    data_first = lax.axis_index(DP) == 0
    local_squares = jnp.sum(grad_in * grad_in) + jnp.sum(grad_out_t * grad_out_t)
    local_squares = local_squares + jnp.where(
        data_first, jnp.sum(grad_conv * grad_conv) + jnp.sum(grad_head * grad_head), 0.0
    )
    col_squares = local_squares
    for axis in reversed(DP):
        col_squares = butterfly_sum(col_squares, axis)
    tail = butterfly_sum(jnp.concatenate([gain_dp, col_squares[None]]), "mp")
    grad_gain = tail[:-1]
    squares = tail[-1] + jnp.sum(grad_gain * grad_gain)
    clip_factor = jnp.minimum(1.0, max_norm / (jnp.sqrt(squares) + 1e-06))

    new_in = adam_update(clip_factor * grad_in, in_master, in_first, in_second, 0.1)
    new_out = adam_update(clip_factor * grad_out_t.T, out_master, out_first, out_second, 0.1)
    new_conv = adam_update(clip_factor * grad_conv, conv_master, conv_first, conv_second, 0.1)
    new_head = adam_update(clip_factor * grad_head, head_master, head_first, head_second, 0.0)
    new_gain = adam_update(clip_factor * grad_gain, gain_master, gain_first, gain_second, 0.0)

    low = jnp.concatenate(
        [new_in[0].astype(jnp.bfloat16), new_out[0].T.astype(jnp.bfloat16)], axis=1
    )
    for axis in DP:
        low = gather_stack(low, axis)
    in_weights = jnp.transpose(low[..., :n_in], (2, 1, 0, 3, 4)).reshape(-1, n_in)
    out_weights = jnp.transpose(low[..., n_in:], (4, 2, 1, 0, 3)).reshape(cols - n_in, -1)
    return (
        new_in[0],
        new_in[1],
        new_in[2],
        in_weights,
        new_out[0],
        new_out[1],
        new_out[2],
        out_weights,
        new_conv[0],
        new_conv[1],
        new_conv[2],
        new_head[0],
        new_head[1],
        new_head[2],
        new_gain[0],
        new_gain[1],
        new_gain[2],
    )


def solution(mesh):
    n_dp, n_mp = mesh.devices.shape
    split = Mesh(mesh.devices.reshape(n_dp // 8, 4, 2, n_mp), DP + ("mp",))
    return jax.shard_map(
        body,
        mesh=split,
        in_specs=(
            P(DP, None),
            P(DP, "mp"),
            P(DP, "mp"),
            P(DP, None),
            P(DP, "mp"),
            P(DP, "mp"),
            P(DP, "mp"),
            P("mp", DP),
            P("mp", DP),
            P("mp", DP),
            P(DP, None, None, "mp"),
            P(None, "mp"),
            P(None, "mp"),
            P(None, "mp"),
            P(DP, None, "mp", None),
            P("mp", None),
            P("mp", None),
            P("mp", None),
            P(DP, None, "mp", None),
            P(),
            P(),
            P(),
        ),
        out_specs=(
            P(DP, "mp"),
            P(DP, "mp"),
            P(DP, "mp"),
            P(None, "mp"),
            P("mp", DP),
            P("mp", DP),
            P("mp", DP),
            P("mp", None),
            P(None, "mp"),
            P(None, "mp"),
            P(None, "mp"),
            P("mp", None),
            P("mp", None),
            P("mp", None),
            P(),
            P(),
            P(),
        ),
        check_vma=False,
    )
```

```python
import jax
import jax.numpy as jnp
from jax import lax
from jax.sharding import Mesh, PartitionSpec as P

beta_one = 0.9
beta_two = 0.95
adam_step = 10
adam_eps = 1e-08
learn_rate = 0.003
max_norm = 1.0


def contract(left, right):
    return lax.dot_general(
        left, right, (((0,), (0,)), ((), ())), preferred_element_type=jnp.float32
    )


def adam_update(gradient, master, first, second, decay):
    first_new = beta_one * first + (1.0 - beta_one) * gradient
    second_new = beta_two * second + (1.0 - beta_two) * gradient * gradient
    ratio = (
        first_new
        / (1.0 - beta_one**adam_step)
        / (jnp.sqrt(second_new / (1.0 - beta_two**adam_step)) + adam_eps)
    )
    return (master - learn_rate * (ratio + decay * master), first_new, second_new)


DP = ("z", "y", "c")


def nested_psum(value, axes):
    for axis in reversed(axes):
        value = lax.psum(value, axis)
    return value


def by_source(pieces, me):
    stacked = jnp.stack(pieces[::-1])
    return jnp.roll(stacked, me + 1, axis=0)


def scatter_sum(value, rows, axis, dim):
    n = lax.axis_size(axis)
    me = lax.axis_index(axis)
    lead = (0,) * (value.ndim - 3)
    total = lax.dynamic_index_in_dim(value, me, dim, keepdims=False)
    smalls = [total[lead][rows:]]
    for shift in range(1, n):
        part = lax.dynamic_index_in_dim(value, (me + shift) % n, dim, keepdims=False)
        pairs = [(j, (j + shift) % n) for j in range(n)]
        got = lax.ppermute(part, axis, pairs)
        total = total + got
        smalls.append(got[lead][rows:])
    small = jnp.sum(by_source(smalls, me), axis=0)
    grad = total[..., :rows, :]
    small = jnp.broadcast_to(small, grad.shape[:-2] + small.shape)
    return jnp.concatenate([grad, small], axis=-2)


def butterfly_sum(value, axis):
    n = lax.axis_size(axis)
    step = 1
    while step < n:
        pairs = [(j, j ^ step) for j in range(n)]
        value = value + lax.ppermute(value, axis, pairs)
        step *= 2
    return value


def gather_stack(value, axis):
    n = lax.axis_size(axis)
    me = lax.axis_index(axis)
    pieces = [value]
    for shift in range(1, n):
        pairs = [(j, (j + shift) % n) for j in range(n)]
        pieces.append(lax.ppermute(value, axis, pairs))
    stacked = jnp.stack(pieces[::-1])
    return jnp.roll(stacked, me + 1, axis=0)


def body(
    acts,
    proj_cotangent,
    inner_acts,
    out_cotangent,
    in_master,
    in_first,
    in_second,
    out_master,
    out_first,
    out_second,
    conv_grads,
    conv_master,
    conv_first,
    conv_second,
    head_grads,
    head_master,
    head_first,
    head_second,
    gain_grads,
    gain_master,
    gain_first,
    gain_second,
):
    n_dp = lax.axis_size(DP)
    width, n_in = acts.shape[1], proj_cotangent.shape[1]
    rows = width // n_dp
    part_in = contract(acts, proj_cotangent)
    part_out = contract(out_cotangent, inner_acts)
    sizes = [lax.axis_size(a) for a in DP]
    both = jnp.concatenate(
        [part_in.reshape(*sizes, rows, -1), part_out.reshape(*sizes, rows, -1)], axis=-1
    )
    cols = both.shape[-1]
    conv_local = jnp.sum(conv_grads, axis=(0, 1))
    head_local = jnp.sum(head_grads, axis=(0, 1))
    gain_local = jnp.sum(gain_grads, axis=(0, 1, 2))
    n_conv, n_head = conv_local.size, head_local.size
    small = jnp.concatenate(
        [conv_local.reshape(-1), head_local.reshape(-1), gain_local]
    )
    n_small = small.size
    small_rows = -(-n_small // cols)
    small = jnp.pad(small, (0, small_rows * cols - n_small)).reshape(small_rows, cols)
    both = jnp.concatenate(
        [both, jnp.broadcast_to(small, both.shape[:-2] + small.shape)], axis=-2
    )
    both = scatter_sum(both, rows, DP[2], 2)
    both = scatter_sum(both, rows, DP[1], 1)
    both = scatter_sum(both, rows, DP[0], 0)
    grad_both = both[:rows]
    small = both[rows:].reshape(-1)[:n_small]
    grad_in = grad_both[:, :n_in]
    grad_out_t = grad_both[:, n_in:]

    grad_conv = small[:n_conv].reshape(conv_local.shape)
    grad_head = small[n_conv : n_conv + n_head].reshape(head_local.shape)
    gain_dp = small[n_conv + n_head :]

    data_first = lax.axis_index(DP) == 0
    local_squares = jnp.sum(grad_in * grad_in) + jnp.sum(grad_out_t * grad_out_t)
    local_squares = local_squares + jnp.where(
        data_first, jnp.sum(grad_conv * grad_conv) + jnp.sum(grad_head * grad_head), 0.0
    )
    col_squares = local_squares
    for axis in reversed(DP):
        col_squares = lax.psum(col_squares, axis) if axis == DP[2] else butterfly_sum(col_squares, axis)
    tail = butterfly_sum(jnp.concatenate([gain_dp, col_squares[None]]), "mp")
    grad_gain = tail[:-1]
    squares = tail[-1] + jnp.sum(grad_gain * grad_gain)
    clip_factor = jnp.minimum(1.0, max_norm / (jnp.sqrt(squares) + 1e-06))

    new_in = adam_update(clip_factor * grad_in, in_master, in_first, in_second, 0.1)
    new_out = adam_update(clip_factor * grad_out_t.T, out_master, out_first, out_second, 0.1)
    new_conv = adam_update(clip_factor * grad_conv, conv_master, conv_first, conv_second, 0.1)
    new_head = adam_update(clip_factor * grad_head, head_master, head_first, head_second, 0.0)
    new_gain = adam_update(clip_factor * grad_gain, gain_master, gain_first, gain_second, 0.0)

    low = jnp.concatenate(
        [new_in[0].astype(jnp.bfloat16), new_out[0].T.astype(jnp.bfloat16)], axis=1
    )
    for axis in DP:
        low = gather_stack(low, axis)
    in_weights = jnp.transpose(low[..., :n_in], (2, 1, 0, 3, 4)).reshape(-1, n_in)
    out_weights = jnp.transpose(low[..., n_in:], (4, 2, 1, 0, 3)).reshape(cols - n_in, -1)
    return (
        new_in[0],
        new_in[1],
        new_in[2],
        in_weights,
        new_out[0],
        new_out[1],
        new_out[2],
        out_weights,
        new_conv[0],
        new_conv[1],
        new_conv[2],
        new_head[0],
        new_head[1],
        new_head[2],
        new_gain[0],
        new_gain[1],
        new_gain[2],
    )


def solution(mesh):
    n_dp, n_mp = mesh.devices.shape
    split = Mesh(mesh.devices.reshape(n_dp // 8, 4, 2, n_mp), DP + ("mp",))
    return jax.shard_map(
        body,
        mesh=split,
        in_specs=(
            P(DP, None),
            P(DP, "mp"),
            P(DP, "mp"),
            P(DP, None),
            P(DP, "mp"),
            P(DP, "mp"),
            P(DP, "mp"),
            P("mp", DP),
            P("mp", DP),
            P("mp", DP),
            P(DP, None, None, "mp"),
            P(None, "mp"),
            P(None, "mp"),
            P(None, "mp"),
            P(DP, None, "mp", None),
            P("mp", None),
            P("mp", None),
            P("mp", None),
            P(DP, None, "mp", None),
            P(),
            P(),
            P(),
        ),
        out_specs=(
            P(DP, "mp"),
            P(DP, "mp"),
            P(DP, "mp"),
            P(None, "mp"),
            P("mp", DP),
            P("mp", DP),
            P("mp", DP),
            P("mp", None),
            P(None, "mp"),
            P(None, "mp"),
            P(None, "mp"),
            P("mp", None),
            P("mp", None),
            P("mp", None),
            P(),
            P(),
            P(),
        ),
        check_vma=False,
    )
```

```python
import jax
import jax.numpy as jnp
from jax import lax
from jax.sharding import Mesh, PartitionSpec as P

beta_one = 0.9
beta_two = 0.95
adam_step = 10
adam_eps = 1e-08
learn_rate = 0.003
max_norm = 1.0


def contract(left, right):
    return lax.dot_general(
        left, right, (((0,), (0,)), ((), ())), preferred_element_type=jnp.float32
    )


def adam_update(gradient, master, first, second, decay):
    first_new = beta_one * first + (1.0 - beta_one) * gradient
    second_new = beta_two * second + (1.0 - beta_two) * gradient * gradient
    ratio = (
        first_new
        / (1.0 - beta_one**adam_step)
        / (jnp.sqrt(second_new / (1.0 - beta_two**adam_step)) + adam_eps)
    )
    return (master - learn_rate * (ratio + decay * master), first_new, second_new)


DP = ("z", "y", "c")


def nested_psum(value, axes):
    for axis in reversed(axes):
        value = lax.psum(value, axis)
    return value


def by_source(pieces, me):
    stacked = jnp.stack(pieces[::-1])
    return jnp.roll(stacked, me + 1, axis=0)


def scatter_sum(value, rows, axis, dim):
    n = lax.axis_size(axis)
    me = lax.axis_index(axis)
    lead = (0,) * (value.ndim - 3)
    total = lax.dynamic_index_in_dim(value, me, dim, keepdims=False)
    smalls = [total[lead][rows:]]
    for shift in range(1, n):
        part = lax.dynamic_index_in_dim(value, (me + shift) % n, dim, keepdims=False)
        pairs = [(j, (j + shift) % n) for j in range(n)]
        got = lax.ppermute(part, axis, pairs)
        total = total + got
        smalls.append(got[lead][rows:])
    small = jnp.sum(by_source(smalls, me), axis=0)
    grad = total[..., :rows, :]
    small = jnp.broadcast_to(small, grad.shape[:-2] + small.shape)
    return jnp.concatenate([grad, small], axis=-2)


def butterfly_sum(value, axis):
    n = lax.axis_size(axis)
    step = 1
    while step < n:
        pairs = [(j, j ^ step) for j in range(n)]
        value = value + lax.ppermute(value, axis, pairs)
        step *= 2
    return value


def gather_stack(value, axis):
    n = lax.axis_size(axis)
    me = lax.axis_index(axis)
    pieces = [value]
    for shift in range(1, n):
        pairs = [(j, (j + shift) % n) for j in range(n)]
        pieces.append(lax.ppermute(value, axis, pairs))
    stacked = jnp.stack(pieces[::-1])
    return jnp.roll(stacked, me + 1, axis=0)


def body(
    acts,
    proj_cotangent,
    inner_acts,
    out_cotangent,
    in_master,
    in_first,
    in_second,
    out_master,
    out_first,
    out_second,
    conv_grads,
    conv_master,
    conv_first,
    conv_second,
    head_grads,
    head_master,
    head_first,
    head_second,
    gain_grads,
    gain_master,
    gain_first,
    gain_second,
):
    n_dp = lax.axis_size(DP)
    width, n_in = acts.shape[1], proj_cotangent.shape[1]
    rows = width // n_dp
    part_in = contract(acts, proj_cotangent)
    part_out = contract(out_cotangent, inner_acts)
    sizes = [lax.axis_size(a) for a in DP]
    both = jnp.concatenate(
        [part_in.reshape(*sizes, rows, -1), part_out.reshape(*sizes, rows, -1)], axis=-1
    )
    cols = both.shape[-1]
    conv_local = jnp.sum(conv_grads, axis=(0, 1))
    head_local = jnp.sum(head_grads, axis=(0, 1))
    gain_local = jnp.sum(gain_grads, axis=(0, 1, 2))
    n_conv, n_head = conv_local.size, head_local.size
    small = jnp.concatenate(
        [conv_local.reshape(-1), head_local.reshape(-1), gain_local]
    )
    n_small = small.size
    small_rows = -(-n_small // cols)
    small = jnp.pad(small, (0, small_rows * cols - n_small)).reshape(small_rows, cols)
    both = jnp.concatenate(
        [both, jnp.broadcast_to(small, both.shape[:-2] + small.shape)], axis=-2
    )
    both = scatter_sum(both, rows, DP[2], 2)
    both = scatter_sum(both, rows, DP[1], 1)
    both = scatter_sum(both, rows, DP[0], 0)
    grad_both = both[:rows]
    small = both[rows:].reshape(-1)[:n_small]
    grad_in = grad_both[:, :n_in]
    grad_out_t = grad_both[:, n_in:]

    grad_conv = small[:n_conv].reshape(conv_local.shape)
    grad_head = small[n_conv : n_conv + n_head].reshape(head_local.shape)
    gain_dp = small[n_conv + n_head :]

    data_first = lax.axis_index(DP) == 0
    local_squares = jnp.sum(grad_in * grad_in) + jnp.sum(grad_out_t * grad_out_t)
    local_squares = local_squares + jnp.where(
        data_first, jnp.sum(grad_conv * grad_conv) + jnp.sum(grad_head * grad_head), 0.0
    )
    col_squares = local_squares
    for axis in reversed(DP):
        col_squares = lax.psum(col_squares, axis) if axis == DP[2] else butterfly_sum(col_squares, axis)
    tail = lax.psum(jnp.concatenate([gain_dp, col_squares[None]]), "mp")
    grad_gain = tail[:-1]
    squares = tail[-1] + jnp.sum(grad_gain * grad_gain)
    clip_factor = jnp.minimum(1.0, max_norm / (jnp.sqrt(squares) + 1e-06))

    new_in = adam_update(clip_factor * grad_in, in_master, in_first, in_second, 0.1)
    new_out = adam_update(clip_factor * grad_out_t.T, out_master, out_first, out_second, 0.1)
    new_conv = adam_update(clip_factor * grad_conv, conv_master, conv_first, conv_second, 0.1)
    new_head = adam_update(clip_factor * grad_head, head_master, head_first, head_second, 0.0)
    new_gain = adam_update(clip_factor * grad_gain, gain_master, gain_first, gain_second, 0.0)

    low = jnp.concatenate(
        [new_in[0].astype(jnp.bfloat16), new_out[0].T.astype(jnp.bfloat16)], axis=1
    )
    for axis in DP:
        low = gather_stack(low, axis)
    in_weights = jnp.transpose(low[..., :n_in], (2, 1, 0, 3, 4)).reshape(-1, n_in)
    out_weights = jnp.transpose(low[..., n_in:], (4, 2, 1, 0, 3)).reshape(cols - n_in, -1)
    return (
        new_in[0],
        new_in[1],
        new_in[2],
        in_weights,
        new_out[0],
        new_out[1],
        new_out[2],
        out_weights,
        new_conv[0],
        new_conv[1],
        new_conv[2],
        new_head[0],
        new_head[1],
        new_head[2],
        new_gain[0],
        new_gain[1],
        new_gain[2],
    )


def solution(mesh):
    n_dp, n_mp = mesh.devices.shape
    split = Mesh(mesh.devices.reshape(n_dp // 8, 4, 2, n_mp), DP + ("mp",))
    return jax.shard_map(
        body,
        mesh=split,
        in_specs=(
            P(DP, None),
            P(DP, "mp"),
            P(DP, "mp"),
            P(DP, None),
            P(DP, "mp"),
            P(DP, "mp"),
            P(DP, "mp"),
            P("mp", DP),
            P("mp", DP),
            P("mp", DP),
            P(DP, None, None, "mp"),
            P(None, "mp"),
            P(None, "mp"),
            P(None, "mp"),
            P(DP, None, "mp", None),
            P("mp", None),
            P("mp", None),
            P("mp", None),
            P(DP, None, "mp", None),
            P(),
            P(),
            P(),
        ),
        out_specs=(
            P(DP, "mp"),
            P(DP, "mp"),
            P(DP, "mp"),
            P(None, "mp"),
            P("mp", DP),
            P("mp", DP),
            P("mp", DP),
            P("mp", None),
            P(None, "mp"),
            P(None, "mp"),
            P(None, "mp"),
            P("mp", None),
            P("mp", None),
            P("mp", None),
            P(),
            P(),
            P(),
        ),
        check_vma=False,
    )
```
